256 devices in a mesh: dp: 32 (over z, x_lo, core), factor: 8 (over y, x_hi).
Axes of the slice: x: 4 (x_hi: 2, x_lo: 2; x = x_hi * 2 + x_lo), y: 4, z: 8, core: 2. Of those that a mesh axis runs over, the one named last changes fastest.
Arguments:
- activations: bfloat16 [65536, 14336], P('dp', 'factor'), may hold values from -6 to 6
- out_grads: bfloat16 [65536, 4096], P('dp', 'factor'), may hold values from -6 to 6
- proj_in: bfloat16 [14336, 256], P('factor'), may hold values from -0.046875 to 0.046875
- proj_out: bfloat16 [4096, 256], P('factor'), may hold values from -0.09375 to 0.09375
- basis_in: bfloat16 [256, 256], replicated, may hold values from -0.375 to 0.375
- basis_out: bfloat16 [256, 256], replicated, may hold values from -0.375 to 0.375
- eigen_values: float32 [256, 256], P('factor'), may hold values from 0.01 to 10
- query_in: bfloat16 [256, 8, 256], P('dp'), may hold values from -3 to 3
- query_out: bfloat16 [256, 8, 256], P('dp'), may hold values from -3 to 3
- lengths: int32 [32, 16], P('dp'), may hold values from 1 to 256, 2048 in all within a row
- continues: int32 [32], replicated, may hold values from 0 to 1, as said below
- owners: int32 [512, 1], replicated, may hold values from 0 to 31; in each aligned block of 512 rows (0 to 511, 512 to 1023, ...) at most 32 rows name the same one
Outputs:
- influence: float32 [1024, 256], P('dp')
The draws below stay inside these ranges and needn't reach their ends.
Inputs may be any that keep to these rules, and one draw needn't show every extreme that they name: `lengths`: each row sums to 2048. `continues`: the flags of sequences 0, 15, 16 and 30 are 1; the flag of the last sequence is not read. `owners`: no dp index owns more than 32 document numbers, and one owns exactly 32.
All inputs are finite; a program needn't handle non-finite values.
Results may differ from the reference program's by a relative error of at most 0.0027.
Values may be sent and summed in bfloat16 or wider, within the bound.
No kernel may reach another device: no remote copies, remote signals or barrier semaphores. Data moves between devices by JAX's collectives and lax.ppermute only.
A program may use at most 64 MiB of HBM per device.

```python
import math
import jax
import jax.numpy as jnp
import numpy as np
from jax import lax

D = 4096
FF = 14336
RANK_IN = 256
RANK_OUT = 256
TOK_DEV = 2048
PIECES = 16
QTOK = 8
TOKENS = 65536
QUERIES = 256
DOC_IDS = 512
OWN_CAP = 32
MOST_LEN = 256
N_DP = 32


def draw_continues(key, part):
    flags = jax.random.randint(key, (N_DP,), 0, 2, dtype=jnp.int32)
    flags = flags.at[0].set(1)
    flags = flags.at[N_DP // 2 - 1].set(1)
    flags = flags.at[N_DP // 2].set(1)
    return flags.at[N_DP - 2].set(1)


def steps_of(key, dims, split, low, top_value):
    loudness, own = 1.0, jax.random.fold_in(key, 6)
    for axis_at, shards_of in split:
        heights = jnp.exp(jax.random.uniform(jax.random.fold_in(own, axis_at), (shards_of,), jnp.float32, low / len(split), top_value / len(split)))
        loudness = loudness * jnp.repeat(heights, dims[axis_at] // shards_of).reshape([-1 if axis == axis_at else 1 for axis in range(len(dims))])
    return loudness


def length_profile(number_of, total, reach, slope):
    portions = [(1 << 20) // math.isqrt(rank ** slope) + 1 for rank in range(2, number_of + 1)]
    surplus, holding = total - reach - (number_of - 1), [1] * (number_of - 1)
    while surplus > 0:
        candidates = [i for i in range(number_of - 1) if holding[i] < reach]
        pool, left = sum([portions[i] for i in candidates]), surplus
        for i in candidates:
            addition = min(reach - holding[i], max(1, left * portions[i] // pool), surplus)
            holding[i] = holding[i] + addition
            surplus = surplus - addition
    return np.array([reach] + holding)


def uneven(stream_key, number_of, total, limit, lean):
    if number_of == 2:
        one = jax.random.randint(stream_key, (), max(1, total - limit), min(limit, total - 1) + 1)
        return jnp.stack([one, total - one])
    sizes = jnp.asarray(length_profile(number_of, total, limit, lean), jnp.int32)
    couples = (number_of - 1) // 2
    donor, sink = sizes[1:1 + 2 * couples:2], sizes[2:2 + 2 * couples:2]
    slack = jnp.minimum(donor - 1, limit - sink)
    shifted = jax.random.randint(jax.random.fold_in(stream_key, 1), (couples,), 0, 1 << 20) % (slack + 1)
    sizes = sizes.at[1:1 + 2 * couples:2].set(donor - shifted).at[2:2 + 2 * couples:2].set(sink + shifted)
    return sizes[jax.random.permutation(jax.random.fold_in(stream_key, 2), number_of)]


def routed_block(stream_key, own, number, rows, amount, top, bound, lean):
    sequence = jax.random.permutation(stream_key, amount)
    crowded, common = portions_of(amount, rows * top, bound, lean, True), portions_of(amount, rows * top, bound, lean, False)
    places = jnp.arange(amount)

    def named(tallies, turn):
        used = int((tallies > 0).sum())
        fixed = max(1, used // 4)
        passed = fixed + (places - fixed + turn * (used - fixed)) % max(1, amount - fixed)
        return jnp.zeros((amount,), jnp.int32).at[sequence[jnp.where(places < fixed, places, passed)]].set(jnp.asarray(tallies, jnp.int32))

    tallies = jnp.where(number % 4 == 0, named(crowded, number // 4), named(common, number - number // 4 - 1))
    mixed = jax.random.permutation(jax.random.fold_in(own, 3), amount)
    giver, receiver = mixed[0:amount // 2 * 2:2], mixed[1:amount // 2 * 2:2]
    margin = jnp.minimum(tallies[giver] - 1, bound - tallies[receiver]) // 2
    margin = jnp.where((giver == sequence[0]) | (receiver == sequence[0]) | (tallies[receiver] == 0), 0, jnp.maximum(margin, 0))
    passed = jax.random.randint(jax.random.fold_in(own, 4), (amount // 2,), 0, 1 << 20) % (margin + 1)
    tallies = tallies.at[giver].add(-passed).at[receiver].add(passed)
    labels = jnp.searchsorted(jnp.cumsum(tallies), jnp.arange(rows * top), side="right").astype(jnp.int32)
    listing = labels.reshape(top, rows).T
    listing = listing[jax.random.permutation(jax.random.fold_in(own, 1), rows)]
    turn = jax.random.randint(jax.random.fold_in(own, 2), (rows, 1), 0, top)
    return jnp.take_along_axis(listing, (jnp.arange(top)[None, :] + turn) % top, axis=1)


def portions_of(count, total, reach, lean, full):
    loads = [(1 << 20) // math.isqrt(standing ** lean) + 1 for standing in range(1, count + 1)]
    largest = reach if full else min(reach, max(-(-total // count), total * loads[0] // sum(loads)))
    least = 1 if total - largest >= count - 1 else 0
    given, surplus = [largest] + [least] * (count - 1), total - largest - least * (count - 1)
    while surplus > 0:
        candidates = [i for i in range(1, count) if given[i] < largest] or [i for i in range(1, count) if given[i] < reach]
        pool, budget = sum([loads[i] for i in candidates]), surplus
        for i in candidates:
            extra = min(reach - given[i], max(1, budget * loads[i] // pool), surplus)
            given[i] = given[i] + extra
            surplus = surplus - extra
    return np.array(given)


def scatter_about(rng, dims, spread, limit, cuts=(), kind=jnp.bfloat16):
    loudness = steps_of(rng, dims, cuts, -0.22, 0.18) if cuts else 1.0
    drawn = jax.random.normal(rng, dims, jnp.float32) * spread * loudness
    return jnp.minimum(jnp.maximum(drawn, -limit), limit).astype(kind)


def setup_inputs(seed: int = 0) -> dict:
    arg_keys = jax.random.split(jax.random.key(seed), 13)
    activations = scatter_about(arg_keys[0], (TOKENS, FF), 1.0, 6.0, ((0, 32), (1, 8)))
    out_grads = scatter_about(arg_keys[1], (TOKENS, D), 1.0, 6.0, ((0, 32), (1, 8)))
    proj_in = scatter_about(arg_keys[2], (FF, RANK_IN), FF ** -0.5, 0.046875, ((0, 8),))
    proj_out = scatter_about(arg_keys[3], (D, RANK_OUT), D ** -0.5, 0.09375, ((0, 8),))
    basis_in = scatter_about(arg_keys[4], (RANK_IN, RANK_IN), RANK_IN ** -0.5, 0.375)
    basis_out = scatter_about(arg_keys[5], (RANK_OUT, RANK_OUT), RANK_OUT ** -0.5, 0.375)
    eigen_values = jnp.clip(jnp.exp(math.log(10.0) - 6.9077553 * jax.random.uniform(arg_keys[6], (RANK_OUT, RANK_IN), jnp.float32) ** steps_of(arg_keys[6], (RANK_OUT, RANK_IN), ((0, 8),), -0.2, 0.2)), 0.01, 10.0)
    query_in = scatter_about(arg_keys[7], (QUERIES, QTOK, RANK_IN), 0.5, 3.0, ((0, 32),))
    query_out = scatter_about(arg_keys[8], (QUERIES, QTOK, RANK_OUT), 0.5, 3.0, ((0, 32),))
    lengths = jax.vmap(lambda own: uneven(own, PIECES, TOK_DEV, MOST_LEN, 2))(jax.random.split(arg_keys[9], N_DP)).reshape((N_DP, PIECES)).astype(jnp.int32)
    continues = draw_continues(jax.random.fold_in(arg_keys[12], 71), 0)
    owners_keys = jax.random.split(jax.random.fold_in(arg_keys[11], 1), DOC_IDS // DOC_IDS)
    owners_turns = jax.random.permutation(jax.random.fold_in(arg_keys[11], 3), DOC_IDS // DOC_IDS)
    owners = jax.vmap(lambda own, number: routed_block(jax.random.fold_in(arg_keys[11], 2), own, number, DOC_IDS, N_DP, 1, OWN_CAP, 2))(owners_keys, owners_turns).reshape((DOC_IDS, 1))
    return dict(activations=activations, out_grads=out_grads, proj_in=proj_in, proj_out=proj_out, basis_in=basis_in, basis_out=basis_out, eigen_values=eigen_values, query_in=query_in, query_out=query_out, lengths=lengths, continues=continues, owners=owners)


DAMPING = 0.1
EPSILON = 1e-06

def piece_grads(rot_out, rot_in, piece_lengths):
    piece_ends = jnp.cumsum(piece_lengths)
    piece_starts = piece_ends - piece_lengths
    position = jnp.arange(TOK_DEV, dtype=jnp.int32)[:, None]
    member = ((position >= piece_starts[None, :]) & (position < piece_ends[None, :])).astype(jnp.float32)
    stacked = (member[:, :, None] * rot_out[:, None, :]).reshape(TOK_DEV, PIECES * RANK_OUT)
    grads_here = lax.dot_general(stacked, rot_in, (((0,), (0,)), ((), ())), precision=lax.Precision.HIGHEST)
    return grads_here.reshape(PIECES, RANK_OUT * RANK_IN)

def reference(activations, out_grads, proj_in, proj_out, basis_in, basis_out, eigen_values, query_in, query_out, lengths, continues, owners):
    in_proj = jnp.dot(activations, proj_in, preferred_element_type=jnp.float32)
    out_proj = jnp.dot(out_grads, proj_out, preferred_element_type=jnp.float32)
    basis_in_wide = basis_in.astype(jnp.float32)
    basis_out_wide = basis_out.astype(jnp.float32)
    rot_in = jnp.dot(in_proj, basis_in_wide, precision=lax.Precision.HIGHEST)
    rot_out = jnp.dot(out_proj, basis_out_wide, precision=lax.Precision.HIGHEST)
    all_pieces = lax.map(lambda packed: piece_grads(packed[0], packed[1], packed[2]), (rot_out.reshape(N_DP, TOK_DEV, RANK_OUT), rot_in.reshape(N_DP, TOK_DEV, RANK_IN), lengths))
    preceding = jnp.concatenate([jnp.zeros((1, RANK_OUT * RANK_IN), jnp.float32), all_pieces[:-1, PIECES - 1]], axis=0)
    joined = continues.astype(jnp.float32)
    not_last = (jnp.arange(N_DP, dtype=jnp.int32) < N_DP - 1).astype(jnp.float32)
    joined_next = joined * not_last
    joined_prev = jnp.concatenate([jnp.zeros((1,), jnp.float32), joined[:-1]])
    all_pieces = all_pieces.at[:, 0].add(joined_prev[:, None] * preceding)
    all_pieces = all_pieces.at[:, PIECES - 1].multiply((1.0 - joined_next)[:, None])
    doc_grad = all_pieces.reshape(DOC_IDS, RANK_OUT * RANK_IN)
    scale = (1.0 / (eigen_values + DAMPING)).reshape(-1)
    self_infl = lax.optimization_barrier(jnp.sum(doc_grad * doc_grad * scale[None, :], axis=1))
    grad_low = doc_grad.astype(jnp.bfloat16)
    q_out = jnp.einsum('qtk,kl->qtl', query_out.astype(jnp.float32), basis_out_wide, precision=lax.Precision.HIGHEST)
    q_in = jnp.einsum('qtk,kl->qtl', query_in.astype(jnp.float32), basis_in_wide, precision=lax.Precision.HIGHEST)
    outer = jnp.einsum('qti,qtj->qij', q_out, q_in, precision=lax.Precision.HIGHEST)
    query_grad = (outer.reshape(QUERIES, RANK_OUT * RANK_IN) * scale[None, :]).astype(jnp.bfloat16)
    raw = lax.dot_general(grad_low, query_grad, (((1,), (1,)), ((), ())), preferred_element_type=jnp.float32)
    relative = raw / jnp.sqrt(self_infl + EPSILON)[:, None]
    own_all = owners[:, 0]
    numbers = jnp.arange(DOC_IDS, dtype=jnp.int32)
    earlier = (own_all[None, :] == own_all[:, None]) & (numbers[None, :] < numbers[:, None])
    rank = lax.optimization_barrier(jnp.sum(earlier.astype(jnp.int32), axis=1)).astype(jnp.int32)
    slot_index = own_all * OWN_CAP + rank
    influence = jnp.zeros((N_DP * OWN_CAP, QUERIES), jnp.float32).at[slot_index].set(relative)
    return influence
```

```python
import jax
import jax.numpy as jnp
from jax import lax
from jax.sharding import PartitionSpec as P

OWN_CAP = 32


DAMPING = 0.1
EPSILON = 1e-06


def from_behind(block, axis, distance):
    devices = range(lax.axis_size(axis))
    route = [(i - distance, i) for i in devices if i - distance in devices]
    return lax.ppermute(block, axis, route)


def butterfly_sum(block, axis):
    size = lax.axis_size(axis)
    step = 1
    while step < size:
        block = block + lax.ppermute(block, axis, [(i, i ^ step) for i in range(size)])
        step *= 2
    return block


def butterfly_gather(block, axis):
    size = lax.axis_size(axis)
    me = lax.axis_index(axis)
    step = 1
    while step < size:
        other = lax.ppermute(block, axis, [(i, i ^ step) for i in range(size)])
        upper = (me // step) % 2 == 1
        block = jnp.where(
            upper,
            jnp.concatenate([other, block], axis=0),
            jnp.concatenate([block, other], axis=0),
        )
        step *= 2
    return block


def per_device(
    activations,
    out_grads,
    proj_in,
    proj_out,
    basis_in,
    basis_out,
    eigen_values,
    query_in,
    query_out,
    lengths,
    continues,
    owners,
):
    tokens_here = activations.shape[0]
    pieces = lengths.shape[1]
    rank_slice = eigen_values.shape[0]
    rank_in = basis_in.shape[0]
    rank_out = basis_out.shape[0]
    factor_index = lax.axis_index("factor")
    factor_count = lax.axis_size("factor")
    data_index = lax.axis_index("dp")
    data_count = lax.axis_size("dp")
    highest = lax.Precision.HIGHEST
    chunk = tokens_here // factor_count

    queries = lax.all_gather(jnp.concatenate([query_in, query_out], axis=2), "dp", axis=0, tiled=True)

    in_part = jnp.dot(activations, proj_in, preferred_element_type=jnp.float32)
    out_part = jnp.dot(out_grads, proj_out, preferred_element_type=jnp.float32)
    stacked_parts = jnp.concatenate([in_part, out_part], axis=1)
    gathered_parts = lax.all_to_all(stacked_parts, "factor", 0, 0, tiled=True)
    chunk_sums = jnp.sum(gathered_parts.reshape(factor_count, chunk, rank_in + rank_out), axis=0)
    basis_in_wide = basis_in.astype(jnp.float32)
    basis_out_wide = basis_out.astype(jnp.float32)
    rot_in_chunk = jnp.dot(chunk_sums[:, :rank_in], basis_in_wide, precision=highest)
    rot_out_chunk = jnp.dot(chunk_sums[:, rank_in:], basis_out_wide, precision=highest)
    out_blocks = rot_out_chunk.reshape(chunk, factor_count, rank_slice).transpose(1, 0, 2)
    sending = jnp.concatenate(
        [jnp.broadcast_to(rot_in_chunk[None], (factor_count, chunk, rank_in)), out_blocks], axis=2
    ).reshape(factor_count * chunk, rank_in + rank_slice)
    received = lax.all_to_all(sending, "factor", 0, 0, tiled=True)
    rot_in = received[:, :rank_in]
    rot_out_rows = received[:, rank_in:]

    piece_lengths = lengths[0]
    piece_ends = jnp.cumsum(piece_lengths)
    piece_starts = piece_ends - piece_lengths
    position = jnp.arange(tokens_here, dtype=jnp.int32)[:, None]
    member = ((position >= piece_starts[None, :]) & (position < piece_ends[None, :])).astype(
        jnp.float32
    )
    stacked = (member[:, :, None] * rot_out_rows[:, None, :]).reshape(
        tokens_here, pieces * rank_slice
    )
    grad_rows = lax.dot_general(stacked, rot_in, (((0,), (0,)), ((), ())), precision=highest)
    grad_rows = grad_rows.reshape(pieces, rank_slice * rank_in)
    preceding = from_behind(grad_rows[pieces - 1], "dp", 1)
    joined_next = jnp.where(data_index < data_count - 1, continues[data_index], 0).astype(
        jnp.float32
    )
    joined_prev = jnp.where(data_index > 0, continues[jnp.maximum(data_index - 1, 0)], 0).astype(
        jnp.float32
    )
    grad_rows = grad_rows.at[0].add(joined_prev * preceding)
    grad_rows = grad_rows.at[pieces - 1].multiply(1.0 - joined_next)
    scale = (1.0 / (eigen_values + DAMPING)).reshape(-1)
    self_part = jnp.sum(grad_rows * grad_rows * scale[None, :], axis=1)
    grad_low = grad_rows.astype(jnp.bfloat16)

    basis_cut = lax.dynamic_slice_in_dim(basis_out_wide, factor_index * rank_slice, rank_slice, 1)
    q_in = jnp.einsum(
        "qtk,kl->qtl", queries[:, :, :rank_in].astype(jnp.float32), basis_in_wide, precision=highest
    )
    q_out = jnp.einsum(
        "qtk,kl->qtl", queries[:, :, rank_in:].astype(jnp.float32), basis_cut, precision=highest
    )
    outer = jnp.einsum("qti,qtj->qij", q_out, q_in, precision=highest)
    query_grad = (outer.reshape(queries.shape[0], rank_slice * rank_in) * scale[None, :]).astype(
        jnp.bfloat16
    )
    part = lax.dot_general(
        grad_low, query_grad, (((1,), (1,)), ((), ())), preferred_element_type=jnp.float32
    )

    totals = butterfly_sum(jnp.concatenate([part, self_part[:, None]], axis=1), "factor")
    relative = totals[:, :-1] / jnp.sqrt(totals[:, -1:] + EPSILON)
    relative_all = butterfly_gather(relative, "dp")

    own_all = owners[:, 0]
    doc_count = own_all.shape[0]
    numbers = jnp.arange(doc_count, dtype=jnp.int32)
    earlier = (own_all[None, :] == own_all[:, None]) & (numbers[None, :] < numbers[:, None])
    rank_all = jnp.sum(earlier.astype(jnp.int32), axis=1)
    slots = jnp.arange(OWN_CAP, dtype=jnp.int32)[:, None]
    placing = ((own_all[None, :] == data_index) & (rank_all[None, :] == slots)).astype(jnp.float32)
    return jnp.dot(placing, relative_all, precision=highest)


def solution(mesh):
    placed = (
        P("dp", "factor"),
        P("dp", "factor"),
        P("factor", None),
        P("factor", None),
        P(),
        P(),
        P("factor", None),
        P("dp", None, None),
        P("dp", None, None),
        P("dp", None),
        P(),
        P(),
    )
    return jax.shard_map(
        per_device, mesh=mesh, in_specs=placed, out_specs=P("dp", None), check_vma=False
    )
```

```python
import jax
import jax.numpy as jnp
from jax import lax
from jax.sharding import PartitionSpec as P

OWN_CAP = 32


DAMPING = 0.1
EPSILON = 1e-06


def from_behind(block, axis, distance):
    devices = range(lax.axis_size(axis))
    route = [(i - distance, i) for i in devices if i - distance in devices]
    return lax.ppermute(block, axis, route)


def butterfly_sum(block, axis):
    size = lax.axis_size(axis)
    step = 1
    while step < size:
        block = block + lax.ppermute(block, axis, [(i, i ^ step) for i in range(size)])
        step *= 2
    return block


def butterfly_gather(block, axis):
    size = lax.axis_size(axis)
    me = lax.axis_index(axis)
    step = size // 2
    while step >= 1:
        other = lax.ppermute(block, axis, [(i, i ^ step) for i in range(size)])
        upper = (me // step) % 2 == 1
        block = jnp.where(
            upper,
            jnp.concatenate([other, block], axis=0),
            jnp.concatenate([block, other], axis=0),
        )
        step //= 2
    return block


def bit_reversed(count):
    width = count.bit_length() - 1
    return [int(format(i, f"0{width}b")[::-1], 2) for i in range(count)]


def per_device(
    activations,
    out_grads,
    proj_in,
    proj_out,
    basis_in,
    basis_out,
    eigen_values,
    query_in,
    query_out,
    lengths,
    continues,
    owners,
):
    tokens_here = activations.shape[0]
    pieces = lengths.shape[1]
    rank_slice = eigen_values.shape[0]
    rank_in = basis_in.shape[0]
    rank_out = basis_out.shape[0]
    factor_index = lax.axis_index("factor")
    factor_count = lax.axis_size("factor")
    data_index = lax.axis_index("dp")
    data_count = lax.axis_size("dp")
    highest = lax.Precision.HIGHEST
    chunk = tokens_here // factor_count


    in_part = jnp.dot(activations, proj_in, preferred_element_type=jnp.float32)
    out_part = jnp.dot(out_grads, proj_out, preferred_element_type=jnp.float32)
    stacked_parts = jnp.concatenate([in_part, out_part], axis=1)
    gathered_parts = lax.all_to_all(stacked_parts, "factor", 0, 0, tiled=True)
    chunk_sums = jnp.sum(gathered_parts.reshape(factor_count, chunk, rank_in + rank_out), axis=0)
    basis_in_wide = basis_in.astype(jnp.float32)
    basis_out_wide = basis_out.astype(jnp.float32)
    rot_in_chunk = jnp.dot(chunk_sums[:, :rank_in], basis_in_wide, precision=highest)
    rot_out_chunk = jnp.dot(chunk_sums[:, rank_in:], basis_out_wide, precision=highest)
    out_blocks = rot_out_chunk.reshape(chunk, factor_count, rank_slice).transpose(1, 0, 2)
    sending = jnp.concatenate(
        [jnp.broadcast_to(rot_in_chunk[None], (factor_count, chunk, rank_in)), out_blocks], axis=2
    ).reshape(factor_count * chunk, rank_in + rank_slice)
    received = lax.all_to_all(sending, "factor", 0, 0, tiled=True)
    rot_in = received[:, :rank_in]
    rot_out_rows = received[:, rank_in:]

    piece_lengths = lengths[0]
    piece_ends = jnp.cumsum(piece_lengths)
    piece_starts = piece_ends - piece_lengths
    position = jnp.arange(tokens_here, dtype=jnp.int32)[:, None]
    member = ((position >= piece_starts[None, :]) & (position < piece_ends[None, :])).astype(
        jnp.float32
    )
    stacked = (member[:, :, None] * rot_out_rows[:, None, :]).reshape(
        tokens_here, pieces * rank_slice
    )
    grad_rows = lax.dot_general(stacked, rot_in, (((0,), (0,)), ((), ())), precision=highest)
    grad_rows = grad_rows.reshape(pieces, rank_slice * rank_in)
    preceding = from_behind(grad_rows[pieces - 1], "dp", 1)
    joined_next = jnp.where(data_index < data_count - 1, continues[data_index], 0).astype(
        jnp.float32
    )
    joined_prev = jnp.where(data_index > 0, continues[jnp.maximum(data_index - 1, 0)], 0).astype(
        jnp.float32
    )
    grad_rows = grad_rows.at[0].add(joined_prev * preceding)
    grad_rows = grad_rows.at[pieces - 1].multiply(1.0 - joined_next)
    scale = (1.0 / (eigen_values + DAMPING)).reshape(-1)
    self_part = jnp.sum(grad_rows * grad_rows * scale[None, :], axis=1)
    grad_low = grad_rows.astype(jnp.bfloat16)

    basis_cut = lax.dynamic_slice_in_dim(basis_out_wide, factor_index * rank_slice, rank_slice, 1)
    q_out = jnp.einsum("qtk,kl->qtl", query_out.astype(jnp.float32), basis_cut, precision=highest)
    q_in = jnp.einsum("qtk,kl->qtl", query_in.astype(jnp.float32), basis_in_wide, precision=highest)
    outer = jnp.einsum("qti,qtj->qij", q_out, q_in, precision=highest)
    query_grad = lax.all_gather(
        (outer.reshape(query_in.shape[0], rank_slice * rank_in) * scale[None, :]).astype(jnp.bfloat16),
        "dp",
        axis=0,
        tiled=True,
    )
    part = lax.dot_general(
        grad_low, query_grad, (((1,), (1,)), ((), ())), preferred_element_type=jnp.float32
    )

    totals = butterfly_sum(jnp.concatenate([part, self_part[:, None]], axis=1), "factor")
    relative = totals[:, :-1] / jnp.sqrt(totals[:, -1:] + EPSILON)
    relative_all = butterfly_gather(relative, "dp")

    own_all = owners[:, 0]
    doc_count = own_all.shape[0]
    numbers = jnp.arange(doc_count, dtype=jnp.int32)
    earlier = (own_all[None, :] == own_all[:, None]) & (numbers[None, :] < numbers[:, None])
    rank_all = jnp.sum(earlier.astype(jnp.int32), axis=1)
    slots = jnp.arange(OWN_CAP, dtype=jnp.int32)[:, None]
    arrival = jnp.asarray(bit_reversed(data_count), jnp.int32)
    order = (arrival[:, None] * pieces + jnp.arange(pieces, dtype=jnp.int32)[None, :]).reshape(-1)
    placing = ((own_all[order][None, :] == data_index) & (rank_all[order][None, :] == slots)).astype(
        jnp.float32
    )
    return jnp.dot(placing, relative_all, precision=highest)


def solution(mesh):
    placed = (
        P("dp", "factor"),
        P("dp", "factor"),
        P("factor", None),
        P("factor", None),
        P(),
        P(),
        P("factor", None),
        P("dp", None, None),
        P("dp", None, None),
        P("dp", None),
        P(),
        P(),
    )
    return jax.shard_map(
        per_device, mesh=mesh, in_specs=placed, out_specs=P("dp", None), check_vma=False
    )
```

```python
import jax
import jax.numpy as jnp
from jax import lax
from jax.sharding import PartitionSpec as P

OWN_CAP = 32


DAMPING = 0.1
EPSILON = 1e-06


def from_behind(block, axis, distance):
    devices = range(lax.axis_size(axis))
    route = [(i - distance, i) for i in devices if i - distance in devices]
    return lax.ppermute(block, axis, route)


def butterfly_sum(block, axis):
    size = lax.axis_size(axis)
    step = 1
    while step < size:
        block = block + lax.ppermute(block, axis, [(i, i ^ step) for i in range(size)])
        step *= 2
    return block


def butterfly_gather(block, axis):
    size = lax.axis_size(axis)
    me = lax.axis_index(axis)
    step = size // 2
    while step >= 1:
        other = lax.ppermute(block, axis, [(i, i ^ step) for i in range(size)])
        upper = (me // step) % 2 == 1
        block = jnp.where(
            upper,
            jnp.concatenate([other, block], axis=0),
            jnp.concatenate([block, other], axis=0),
        )
        step //= 2
    return block


def per_device(
    activations,
    out_grads,
    proj_in,
    proj_out,
    basis_in,
    basis_out,
    eigen_values,
    query_in,
    query_out,
    lengths,
    continues,
    owners,
):
    tokens_here = activations.shape[0]
    pieces = lengths.shape[1]
    rank_slice = eigen_values.shape[0]
    rank_in = basis_in.shape[0]
    rank_out = basis_out.shape[0]
    factor_index = lax.axis_index("factor")
    factor_count = lax.axis_size("factor")
    data_index = lax.axis_index("dp")
    data_count = lax.axis_size("dp")
    highest = lax.Precision.HIGHEST
    chunk = tokens_here // factor_count


    basis_in_wide = basis_in.astype(jnp.float32)
    basis_out_wide = basis_out.astype(jnp.float32)
    in_part = jnp.dot(activations, proj_in, preferred_element_type=jnp.float32)
    out_part = jnp.dot(out_grads, proj_out, preferred_element_type=jnp.float32)
    rot_out_part = jnp.dot(out_part, basis_out_wide, precision=highest)
    out_cols = rot_out_part.reshape(tokens_here, factor_count, rank_slice).transpose(1, 0, 2)
    in_rows = in_part.reshape(factor_count, chunk, rank_in)
    sending = jnp.concatenate(
        [out_cols.reshape(factor_count, -1), in_rows.reshape(factor_count, -1)], axis=1
    )
    gathered = jnp.sum(lax.all_to_all(sending, "factor", 0, 0, tiled=True), axis=0)
    rot_out_rows = gathered[: tokens_here * rank_slice].reshape(tokens_here, rank_slice)
    in_chunk = gathered[tokens_here * rank_slice :].reshape(chunk, rank_in)
    rot_in_chunk = jnp.dot(in_chunk, basis_in_wide, precision=highest)
    rot_in = lax.all_to_all(
        jnp.broadcast_to(rot_in_chunk[None], (factor_count, chunk, rank_in)).reshape(
            factor_count * chunk, rank_in
        ),
        "factor",
        0,
        0,
        tiled=True,
    )

    piece_lengths = lengths[0]
    piece_ends = jnp.cumsum(piece_lengths)
    piece_starts = piece_ends - piece_lengths
    position = jnp.arange(tokens_here, dtype=jnp.int32)[:, None]
    member = ((position >= piece_starts[None, :]) & (position < piece_ends[None, :])).astype(
        jnp.float32
    )
    stacked = (member[:, :, None] * rot_out_rows[:, None, :]).reshape(
        tokens_here, pieces * rank_slice
    )
    grad_rows = lax.dot_general(stacked, rot_in, (((0,), (0,)), ((), ())), precision=highest)
    grad_rows = grad_rows.reshape(pieces, rank_slice * rank_in)
    preceding = from_behind(grad_rows[pieces - 1], "dp", 1)
    joined_next = jnp.where(data_index < data_count - 1, continues[data_index], 0).astype(
        jnp.float32
    )
    joined_prev = jnp.where(data_index > 0, continues[jnp.maximum(data_index - 1, 0)], 0).astype(
        jnp.float32
    )
    grad_rows = grad_rows.at[0].add(joined_prev * preceding)
    grad_rows = grad_rows.at[pieces - 1].multiply(1.0 - joined_next)
    scale = (1.0 / (eigen_values + DAMPING)).reshape(-1)
    self_part = jnp.sum(grad_rows * grad_rows * scale[None, :], axis=1)
    grad_low = grad_rows.astype(jnp.bfloat16)

    basis_cut = lax.dynamic_slice_in_dim(basis_out_wide, factor_index * rank_slice, rank_slice, 1)
    q_out = jnp.einsum("qtk,kl->qtl", query_out.astype(jnp.float32), basis_cut, precision=highest)
    q_in = jnp.einsum("qtk,kl->qtl", query_in.astype(jnp.float32), basis_in_wide, precision=highest)
    outer = jnp.einsum("qti,qtj->qij", q_out, q_in, precision=highest)
    query_grad = lax.all_gather(
        (outer.reshape(query_in.shape[0], rank_slice * rank_in) * scale[None, :]).astype(jnp.bfloat16),
        "dp",
        axis=0,
        tiled=True,
    )
    part = lax.dot_general(
        grad_low, query_grad, (((1,), (1,)), ((), ())), preferred_element_type=jnp.float32
    )

    totals = butterfly_sum(jnp.concatenate([part, self_part[:, None]], axis=1), "factor")
    relative = totals[:, :-1] / jnp.sqrt(totals[:, -1:] + EPSILON)
    relative_all = butterfly_gather(relative, "dp")

    own_all = owners[:, 0]
    doc_count = own_all.shape[0]
    numbers = jnp.arange(doc_count, dtype=jnp.int32)
    earlier = (own_all[None, :] == own_all[:, None]) & (numbers[None, :] < numbers[:, None])
    rank_all = jnp.sum(earlier.astype(jnp.int32), axis=1)
    slots = jnp.arange(OWN_CAP, dtype=jnp.int32)[:, None]
    bits = data_count.bit_length() - 1
    twisted = tuple(range(bits - 1, -1, -1)) + (bits,)
    own_arrived = own_all.reshape((2,) * bits + (pieces,)).transpose(twisted).reshape(-1)
    rank_arrived = rank_all.reshape((2,) * bits + (pieces,)).transpose(twisted).reshape(-1)
    placing = ((own_arrived[None, :] == data_index) & (rank_arrived[None, :] == slots)).astype(
        jnp.float32
    )
    return jnp.dot(placing, relative_all, precision=highest)


def solution(mesh):
    placed = (
        P("dp", "factor"),
        P("dp", "factor"),
        P("factor", None),
        P("factor", None),
        P(),
        P(),
        P("factor", None),
        P("dp", None, None),
        P("dp", None, None),
        P("dp", None),
        P(),
        P(),
    )
    return jax.shard_map(
        per_device, mesh=mesh, in_specs=placed, out_specs=P("dp", None), check_vma=False
    )
```

```python
import jax
import jax.numpy as jnp
from jax import lax
from jax.sharding import PartitionSpec as P

OWN_CAP = 32


DAMPING = 0.1
EPSILON = 1e-06


def from_behind(block, axis, distance):
    devices = range(lax.axis_size(axis))
    route = [(i - distance, i) for i in devices if i - distance in devices]
    return lax.ppermute(block, axis, route)


def butterfly_sum(block, axis):
    size = lax.axis_size(axis)
    step = 1
    while step < size:
        block = block + lax.ppermute(block, axis, [(i, i ^ step) for i in range(size)])
        step *= 2
    return block


def butterfly_gather(block, axis):
    size = lax.axis_size(axis)
    me = lax.axis_index(axis)
    step = size // 2
    while step >= 1:
        other = lax.ppermute(block, axis, [(i, i ^ step) for i in range(size)])
        upper = (me // step) % 2 == 1
        block = jnp.where(
            upper,
            jnp.concatenate([other, block], axis=0),
            jnp.concatenate([block, other], axis=0),
        )
        step //= 2
    return block


def bit_reversed(rows, count):
    bits = count.bit_length() - 1
    shaped = rows.reshape((2,) * bits + (rows.shape[0] // count,) + rows.shape[1:])
    twisted = tuple(range(bits - 1, -1, -1)) + tuple(range(bits, shaped.ndim))
    return shaped.transpose(twisted).reshape(rows.shape)


def per_device(
    activations,
    out_grads,
    proj_in,
    proj_out,
    basis_in,
    basis_out,
    eigen_values,
    query_in,
    query_out,
    lengths,
    continues,
    owners,
):
    tokens_here = activations.shape[0]
    pieces = lengths.shape[1]
    rank_slice = eigen_values.shape[0]
    rank_in = basis_in.shape[0]
    rank_out = basis_out.shape[0]
    factor_index = lax.axis_index("factor")
    factor_count = lax.axis_size("factor")
    data_index = lax.axis_index("dp")
    data_count = lax.axis_size("dp")
    highest = lax.Precision.HIGHEST
    chunk = tokens_here // factor_count


    in_part = jnp.dot(activations, proj_in, preferred_element_type=jnp.float32)
    out_part = jnp.dot(out_grads, proj_out, preferred_element_type=jnp.float32)
    stacked_parts = jnp.concatenate([in_part, out_part], axis=1)
    gathered_parts = lax.all_to_all(stacked_parts, "factor", 0, 0, tiled=True)
    chunk_sums = jnp.sum(gathered_parts.reshape(factor_count, chunk, rank_in + rank_out), axis=0)
    basis_in_wide = basis_in.astype(jnp.float32)
    basis_out_wide = basis_out.astype(jnp.float32)
    rot_in_chunk = jnp.dot(chunk_sums[:, :rank_in], basis_in_wide, precision=highest)
    rot_out_chunk = jnp.dot(chunk_sums[:, rank_in:], basis_out_wide, precision=highest)
    out_blocks = rot_out_chunk.reshape(chunk, factor_count, rank_slice).transpose(1, 0, 2)
    sending = jnp.concatenate(
        [jnp.broadcast_to(rot_in_chunk[None], (factor_count, chunk, rank_in)), out_blocks], axis=2
    ).reshape(factor_count * chunk, rank_in + rank_slice)
    received = lax.all_to_all(sending, "factor", 0, 0, tiled=True)
    rot_in = received[:, :rank_in]
    rot_out_rows = received[:, rank_in:]

    piece_lengths = lengths[0]
    piece_ends = jnp.cumsum(piece_lengths)
    piece_starts = piece_ends - piece_lengths
    position = jnp.arange(tokens_here, dtype=jnp.int32)[:, None]
    member = ((position >= piece_starts[None, :]) & (position < piece_ends[None, :])).astype(
        jnp.float32
    )
    stacked = (member[:, :, None] * rot_out_rows[:, None, :]).reshape(
        tokens_here, pieces * rank_slice
    )
    grad_rows = lax.dot_general(stacked, rot_in, (((0,), (0,)), ((), ())), precision=highest)
    grad_rows = grad_rows.reshape(pieces, rank_slice * rank_in)
    preceding = from_behind(grad_rows[pieces - 1], "dp", 1)
    joined_next = jnp.where(data_index < data_count - 1, continues[data_index], 0).astype(
        jnp.float32
    )
    joined_prev = jnp.where(data_index > 0, continues[jnp.maximum(data_index - 1, 0)], 0).astype(
        jnp.float32
    )
    grad_rows = grad_rows.at[0].add(joined_prev * preceding)
    grad_rows = grad_rows.at[pieces - 1].multiply(1.0 - joined_next)
    scale = (1.0 / (eigen_values + DAMPING)).reshape(-1)
    self_part = jnp.sum(grad_rows * grad_rows * scale[None, :], axis=1)
    grad_low = grad_rows.astype(jnp.bfloat16)

    basis_cut = lax.dynamic_slice_in_dim(basis_out_wide, factor_index * rank_slice, rank_slice, 1)
    q_out = jnp.einsum("qtk,kl->qtl", query_out.astype(jnp.float32), basis_cut, precision=highest)
    q_in = jnp.einsum("qtk,kl->qtl", query_in.astype(jnp.float32), basis_in_wide, precision=highest)
    outer = jnp.einsum("qti,qtj->qij", q_out, q_in, precision=highest)
    query_grad = butterfly_gather(
        (outer.reshape(query_in.shape[0], rank_slice * rank_in) * scale[None, :]).astype(jnp.bfloat16),
        "dp",
    )
    part = lax.dot_general(
        grad_low, query_grad, (((1,), (1,)), ((), ())), preferred_element_type=jnp.float32
    )
    part = bit_reversed(part.T, data_count).T

    totals = butterfly_sum(jnp.concatenate([part, self_part[:, None]], axis=1), "factor")
    relative = totals[:, :-1] / jnp.sqrt(totals[:, -1:] + EPSILON)
    relative_all = butterfly_gather(relative, "dp")

    own_all = owners[:, 0]
    doc_count = own_all.shape[0]
    numbers = jnp.arange(doc_count, dtype=jnp.int32)
    earlier = (own_all[None, :] == own_all[:, None]) & (numbers[None, :] < numbers[:, None])
    rank_all = jnp.sum(earlier.astype(jnp.int32), axis=1)
    slots = jnp.arange(OWN_CAP, dtype=jnp.int32)[:, None]
    own_arrived = bit_reversed(own_all, data_count)
    rank_arrived = bit_reversed(rank_all, data_count)
    placing = ((own_arrived[None, :] == data_index) & (rank_arrived[None, :] == slots)).astype(
        jnp.float32
    )
    return jnp.dot(placing, relative_all, precision=highest)


def solution(mesh):
    placed = (
        P("dp", "factor"),
        P("dp", "factor"),
        P("factor", None),
        P("factor", None),
        P(),
        P(),
        P("factor", None),
        P("dp", None, None),
        P("dp", None, None),
        P("dp", None),
        P(),
        P(),
    )
    return jax.shard_map(
        per_device, mesh=mesh, in_specs=placed, out_specs=P("dp", None), check_vma=False
    )
```

```python
import jax
import jax.numpy as jnp
from jax import lax
from jax.sharding import PartitionSpec as P

OWN_CAP = 32


DAMPING = 0.1
EPSILON = 1e-06


def from_behind(block, axis, distance):
    devices = range(lax.axis_size(axis))
    route = [(i - distance, i) for i in devices if i - distance in devices]
    return lax.ppermute(block, axis, route)


def butterfly_sum(block, axis):
    size = lax.axis_size(axis)
    step = 1
    while step < size:
        block = block + lax.ppermute(block, axis, [(i, i ^ step) for i in range(size)])
        step *= 2
    return block


def butterfly_gather(block, axis):
    size = lax.axis_size(axis)
    me = lax.axis_index(axis)
    step = size // 2
    while step >= 1:
        other = lax.ppermute(block, axis, [(i, i ^ step) for i in range(size)])
        upper = (me // step) % 2 == 1
        block = jnp.where(
            upper,
            jnp.concatenate([other, block], axis=0),
            jnp.concatenate([block, other], axis=0),
        )
        step //= 2
    return block


def bit_reversed(rows, count):
    bits = count.bit_length() - 1
    shaped = rows.reshape((2,) * bits + (rows.shape[0] // count,) + rows.shape[1:])
    twisted = tuple(range(bits - 1, -1, -1)) + tuple(range(bits, shaped.ndim))
    return shaped.transpose(twisted).reshape(rows.shape)


def per_device(
    activations,
    out_grads,
    proj_in,
    proj_out,
    basis_in,
    basis_out,
    eigen_values,
    query_in,
    query_out,
    lengths,
    continues,
    owners,
):
    tokens_here = activations.shape[0]
    pieces = lengths.shape[1]
    rank_slice = eigen_values.shape[0]
    rank_in = basis_in.shape[0]
    rank_out = basis_out.shape[0]
    factor_index = lax.axis_index("factor")
    factor_count = lax.axis_size("factor")
    data_index = lax.axis_index("dp")
    data_count = lax.axis_size("dp")
    highest = lax.Precision.HIGHEST
    chunk = tokens_here // factor_count
    scale = (1.0 / (eigen_values + DAMPING)).reshape(-1)
    queries = butterfly_gather(jnp.concatenate([query_in, query_out], axis=2), "dp")


    in_part = jnp.dot(activations, proj_in, preferred_element_type=jnp.float32)
    out_part = jnp.dot(out_grads, proj_out, preferred_element_type=jnp.float32)
    stacked_parts = jnp.concatenate([in_part, out_part], axis=1)
    gathered_parts = lax.all_to_all(stacked_parts, "factor", 0, 0, tiled=True)
    chunk_sums = jnp.sum(gathered_parts.reshape(factor_count, chunk, rank_in + rank_out), axis=0)
    basis_in_wide = basis_in.astype(jnp.float32)
    basis_out_wide = basis_out.astype(jnp.float32)
    rot_in_chunk = jnp.dot(chunk_sums[:, :rank_in], basis_in_wide, precision=highest)
    rot_out_chunk = jnp.dot(chunk_sums[:, rank_in:], basis_out_wide, precision=highest)
    out_blocks = rot_out_chunk.reshape(chunk, factor_count, rank_slice).transpose(1, 0, 2)
    sending = jnp.concatenate(
        [jnp.broadcast_to(rot_in_chunk[None], (factor_count, chunk, rank_in)), out_blocks], axis=2
    ).reshape(factor_count * chunk, rank_in + rank_slice)
    received = lax.all_to_all(sending, "factor", 0, 0, tiled=True)
    rot_in = received[:, :rank_in]
    rot_out_rows = received[:, rank_in:]

    piece_lengths = lengths[0]
    piece_ends = jnp.cumsum(piece_lengths)
    piece_starts = piece_ends - piece_lengths
    position = jnp.arange(tokens_here, dtype=jnp.int32)[:, None]
    member = ((position >= piece_starts[None, :]) & (position < piece_ends[None, :])).astype(
        jnp.float32
    )
    stacked = (member[:, :, None] * rot_out_rows[:, None, :]).reshape(
        tokens_here, pieces * rank_slice
    )
    grad_rows = lax.dot_general(stacked, rot_in, (((0,), (0,)), ((), ())), precision=highest)
    grad_rows = grad_rows.reshape(pieces, rank_slice * rank_in)
    preceding = from_behind(grad_rows[pieces - 1], "dp", 1)
    joined_next = jnp.where(data_index < data_count - 1, continues[data_index], 0).astype(
        jnp.float32
    )
    joined_prev = jnp.where(data_index > 0, continues[jnp.maximum(data_index - 1, 0)], 0).astype(
        jnp.float32
    )
    grad_rows = grad_rows.at[0].add(joined_prev * preceding)
    grad_rows = grad_rows.at[pieces - 1].multiply(1.0 - joined_next)
    self_part = jnp.sum(grad_rows * grad_rows * scale[None, :], axis=1)
    grad_low = grad_rows.astype(jnp.bfloat16)

    basis_cut = lax.dynamic_slice_in_dim(basis_out_wide, factor_index * rank_slice, rank_slice, 1)
    q_in = jnp.einsum(
        "qtk,kl->qtl", queries[:, :, :rank_in].astype(jnp.float32), basis_in_wide, precision=highest
    )
    q_out = jnp.einsum(
        "qtk,kl->qtl", queries[:, :, rank_in:].astype(jnp.float32), basis_cut, precision=highest
    )
    outer = jnp.einsum("qti,qtj->qij", q_out, q_in, precision=highest)
    query_grad = (outer.reshape(queries.shape[0], rank_slice * rank_in) * scale[None, :]).astype(
        jnp.bfloat16
    )
    part = lax.dot_general(
        grad_low, query_grad, (((1,), (1,)), ((), ())), preferred_element_type=jnp.float32
    )
    part = bit_reversed(part.T, data_count).T

    totals = butterfly_sum(jnp.concatenate([part, self_part[:, None]], axis=1), "factor")
    relative = totals[:, :-1] / jnp.sqrt(totals[:, -1:] + EPSILON)
    relative_all = butterfly_gather(relative, "dp")

    own_all = owners[:, 0]
    doc_count = own_all.shape[0]
    numbers = jnp.arange(doc_count, dtype=jnp.int32)
    earlier = (own_all[None, :] == own_all[:, None]) & (numbers[None, :] < numbers[:, None])
    rank_all = jnp.sum(earlier.astype(jnp.int32), axis=1)
    slots = jnp.arange(OWN_CAP, dtype=jnp.int32)[:, None]
    own_arrived = bit_reversed(own_all, data_count)
    rank_arrived = bit_reversed(rank_all, data_count)
    placing = ((own_arrived[None, :] == data_index) & (rank_arrived[None, :] == slots)).astype(
        jnp.float32
    )
    return jnp.dot(placing, relative_all, precision=highest)


def solution(mesh):
    placed = (
        P("dp", "factor"),
        P("dp", "factor"),
        P("factor", None),
        P("factor", None),
        P(),
        P(),
        P("factor", None),
        P("dp", None, None),
        P("dp", None, None),
        P("dp", None),
        P(),
        P(),
    )
    return jax.shard_map(
        per_device, mesh=mesh, in_specs=placed, out_specs=P("dp", None), check_vma=False
    )
```

```python
import jax
import jax.numpy as jnp
from jax import lax
from jax.sharding import PartitionSpec as P

OWN_CAP = 32


DAMPING = 0.1
EPSILON = 1e-06


def from_behind(block, axis, distance):
    devices = range(lax.axis_size(axis))
    route = [(i - distance, i) for i in devices if i - distance in devices]
    return lax.ppermute(block, axis, route)


def butterfly_sum(block, axis):
    size = lax.axis_size(axis)
    step = 1
    while step < size:
        block = block + lax.ppermute(block, axis, [(i, i ^ step) for i in range(size)])
        step *= 2
    return block


def butterfly_gather(block, axis):
    size = lax.axis_size(axis)
    me = lax.axis_index(axis)
    step = size // 2
    while step >= 1:
        other = lax.ppermute(block, axis, [(i, i ^ step) for i in range(size)])
        upper = (me // step) % 2 == 1
        block = jnp.where(
            upper,
            jnp.concatenate([other, block], axis=0),
            jnp.concatenate([block, other], axis=0),
        )
        step //= 2
    return block


def bit_reversed(rows, count):
    bits = count.bit_length() - 1
    shaped = rows.reshape((2,) * bits + (rows.shape[0] // count,) + rows.shape[1:])
    twisted = tuple(range(bits - 1, -1, -1)) + tuple(range(bits, shaped.ndim))
    return shaped.transpose(twisted).reshape(rows.shape)


def per_device(
    activations,
    out_grads,
    proj_in,
    proj_out,
    basis_in,
    basis_out,
    eigen_values,
    query_in,
    query_out,
    lengths,
    continues,
    owners,
):
    tokens_here = activations.shape[0]
    pieces = lengths.shape[1]
    rank_slice = eigen_values.shape[0]
    rank_in = basis_in.shape[0]
    rank_out = basis_out.shape[0]
    factor_index = lax.axis_index("factor")
    factor_count = lax.axis_size("factor")
    data_index = lax.axis_index("dp")
    data_count = lax.axis_size("dp")
    highest = lax.Precision.HIGHEST
    chunk = tokens_here // factor_count
    scale_block = 1.0 / (eigen_values + DAMPING)
    queries = butterfly_gather(jnp.concatenate([query_in, query_out], axis=2), "dp")


    basis_in_wide = basis_in.astype(jnp.float32)
    basis_out_wide = basis_out.astype(jnp.float32)
    in_part = jnp.dot(activations, proj_in, preferred_element_type=jnp.float32)
    out_part = jnp.dot(out_grads, proj_out, preferred_element_type=jnp.float32)
    stacked_parts = jnp.concatenate([in_part, out_part], axis=1)
    gathered_parts = lax.all_to_all(stacked_parts, "factor", 0, 0, tiled=True)
    basis_cut = lax.dynamic_slice_in_dim(basis_out_wide, factor_index * rank_slice, rank_slice, 1)
    q_in = jnp.einsum(
        "qtk,kl->qtl", queries[:, :, :rank_in].astype(jnp.float32), basis_in_wide, precision=highest
    )
    q_out = jnp.einsum(
        "qtk,kl->qtl", queries[:, :, rank_in:].astype(jnp.float32), basis_cut, precision=highest
    )
    outer = jnp.einsum("qti,qtj->qij", q_out, q_in, precision=highest)
    query_grad = (outer * scale_block[None]).astype(jnp.bfloat16)
    gathered_parts, query_grad = lax.optimization_barrier((gathered_parts, query_grad))
    chunk_sums = jnp.sum(gathered_parts.reshape(factor_count, chunk, rank_in + rank_out), axis=0)
    rot_in_chunk = jnp.dot(chunk_sums[:, :rank_in], basis_in_wide, precision=highest)
    rot_out_chunk = jnp.dot(chunk_sums[:, rank_in:], basis_out_wide, precision=highest)
    out_blocks = rot_out_chunk.reshape(chunk, factor_count, rank_slice).transpose(1, 0, 2)
    sending = jnp.concatenate(
        [jnp.broadcast_to(rot_in_chunk[None], (factor_count, chunk, rank_in)), out_blocks], axis=2
    ).reshape(factor_count * chunk, rank_in + rank_slice)
    received = lax.all_to_all(sending, "factor", 0, 0, tiled=True)
    rot_in = received[:, :rank_in]
    rot_out_rows = received[:, rank_in:]

    piece_lengths = lengths[0]
    piece_ends = jnp.cumsum(piece_lengths)
    piece_starts = piece_ends - piece_lengths
    position = jnp.arange(tokens_here, dtype=jnp.int32)[:, None]
    member = ((position >= piece_starts[None, :]) & (position < piece_ends[None, :])).astype(
        jnp.float32
    )
    stacked = (member[:, :, None] * rot_out_rows[:, None, :]).reshape(
        tokens_here, pieces * rank_slice
    )
    grad_rows = lax.dot_general(stacked, rot_in, (((0,), (0,)), ((), ())), precision=highest)
    grad_rows = grad_rows.reshape(pieces, rank_slice, rank_in)
    preceding = from_behind(grad_rows[pieces - 1], "dp", 1)
    joined_next = jnp.where(data_index < data_count - 1, continues[data_index], 0).astype(
        jnp.float32
    )
    joined_prev = jnp.where(data_index > 0, continues[jnp.maximum(data_index - 1, 0)], 0).astype(
        jnp.float32
    )
    grad_rows = grad_rows.at[0].add(joined_prev * preceding)
    grad_rows = grad_rows.at[pieces - 1].multiply(1.0 - joined_next)
    self_part = jnp.sum(grad_rows * grad_rows * scale_block[None], axis=(1, 2))
    grad_low = grad_rows.astype(jnp.bfloat16)

    part = lax.dot_general(
        grad_low, query_grad, (((1, 2), (1, 2)), ((), ())), preferred_element_type=jnp.float32
    )
    part = bit_reversed(part.T, data_count).T

    totals = butterfly_sum(jnp.concatenate([part, self_part[:, None]], axis=1), "factor")
    relative = totals[:, :-1] / jnp.sqrt(totals[:, -1:] + EPSILON)
    relative_all = butterfly_gather(relative, "dp")

    own_all = owners[:, 0]
    doc_count = own_all.shape[0]
    numbers = jnp.arange(doc_count, dtype=jnp.int32)
    earlier = (own_all[None, :] == own_all[:, None]) & (numbers[None, :] < numbers[:, None])
    rank_all = jnp.sum(earlier.astype(jnp.int32), axis=1)
    slots = jnp.arange(OWN_CAP, dtype=jnp.int32)[:, None]
    own_arrived = bit_reversed(own_all, data_count)
    rank_arrived = bit_reversed(rank_all, data_count)
    placing = ((own_arrived[None, :] == data_index) & (rank_arrived[None, :] == slots)).astype(
        jnp.float32
    )
    return jnp.dot(placing, relative_all, precision=highest)


def solution(mesh):
    placed = (
        P("dp", "factor"),
        P("dp", "factor"),
        P("factor", None),
        P("factor", None),
        P(),
        P(),
        P("factor", None),
        P("dp", None, None),
        P("dp", None, None),
        P("dp", None),
        P(),
        P(),
    )
    return jax.shard_map(
        per_device, mesh=mesh, in_specs=placed, out_specs=P("dp", None), check_vma=False
    )
```

```python
import jax
import jax.numpy as jnp
from jax import lax
from jax.sharding import PartitionSpec as P

OWN_CAP = 32


DAMPING = 0.1
EPSILON = 1e-06


def from_behind(block, axis, distance):
    devices = range(lax.axis_size(axis))
    route = [(i - distance, i) for i in devices if i - distance in devices]
    return lax.ppermute(block, axis, route)


def butterfly_sum(block, axis):
    size = lax.axis_size(axis)
    step = 1
    while step < size:
        block = block + lax.ppermute(block, axis, [(i, i ^ step) for i in range(size)])
        step *= 2
    return block


def butterfly_gather(block, axis):
    size = lax.axis_size(axis)
    me = lax.axis_index(axis)
    step = size // 2
    while step >= 1:
        other = lax.ppermute(block, axis, [(i, i ^ step) for i in range(size)])
        upper = (me // step) % 2 == 1
        block = jnp.where(
            upper,
            jnp.concatenate([other, block], axis=0),
            jnp.concatenate([block, other], axis=0),
        )
        step //= 2
    return block


def bit_reversed(rows, count):
    bits = count.bit_length() - 1
    shaped = rows.reshape((2,) * bits + (rows.shape[0] // count,) + rows.shape[1:])
    twisted = tuple(range(bits - 1, -1, -1)) + tuple(range(bits, shaped.ndim))
    return shaped.transpose(twisted).reshape(rows.shape)


def per_device(
    activations,
    out_grads,
    proj_in,
    proj_out,
    basis_in,
    basis_out,
    eigen_values,
    query_in,
    query_out,
    lengths,
    continues,
    owners,
):
    tokens_here = activations.shape[0]
    pieces = lengths.shape[1]
    rank_slice = eigen_values.shape[0]
    rank_in = basis_in.shape[0]
    rank_out = basis_out.shape[0]
    factor_index = lax.axis_index("factor")
    factor_count = lax.axis_size("factor")
    data_index = lax.axis_index("dp")
    data_count = lax.axis_size("dp")
    highest = lax.Precision.HIGHEST
    chunk = tokens_here // factor_count
    scale_block = 1.0 / (eigen_values + DAMPING)
    queries = butterfly_gather(jnp.concatenate([query_in, query_out], axis=2), "dp")


    basis_in_wide = basis_in.astype(jnp.float32)
    basis_out_wide = basis_out.astype(jnp.float32)
    in_part = jnp.dot(activations, proj_in, preferred_element_type=jnp.float32)
    out_part = jnp.dot(out_grads, proj_out, preferred_element_type=jnp.float32)
    stacked_parts = jnp.concatenate([in_part, out_part], axis=1)
    gathered_parts = lax.all_to_all(stacked_parts, "factor", 0, 0, tiled=True)
    basis_cut = lax.dynamic_slice_in_dim(basis_out_wide, factor_index * rank_slice, rank_slice, 1)
    q_in = jnp.einsum(
        "qtk,kl->qtl", queries[:, :, :rank_in].astype(jnp.float32), basis_in_wide, precision=highest
    )
    q_out = jnp.einsum(
        "qtk,kl->qtl", queries[:, :, rank_in:].astype(jnp.float32), basis_cut, precision=highest
    )
    outer = jnp.einsum("qti,qtj->qij", q_out, q_in, precision=highest)
    query_grad = (outer * scale_block[None]).astype(jnp.bfloat16)
    chunk_sums = jnp.sum(gathered_parts.reshape(factor_count, chunk, rank_in + rank_out), axis=0)
    rot_in_chunk = jnp.dot(chunk_sums[:, :rank_in], basis_in_wide, precision=highest)
    rot_out_chunk = jnp.dot(chunk_sums[:, rank_in:], basis_out_wide, precision=highest)
    out_blocks = rot_out_chunk.reshape(chunk, factor_count, rank_slice).transpose(1, 0, 2)
    sending = jnp.concatenate(
        [jnp.broadcast_to(rot_in_chunk[None], (factor_count, chunk, rank_in)), out_blocks], axis=2
    ).reshape(factor_count * chunk, rank_in + rank_slice)
    received = lax.all_to_all(sending, "factor", 0, 0, tiled=True)
    rot_in = received[:, :rank_in]
    rot_out_rows = received[:, rank_in:]

    piece_lengths = lengths[0]
    piece_ends = jnp.cumsum(piece_lengths)
    piece_starts = piece_ends - piece_lengths
    position = jnp.arange(tokens_here, dtype=jnp.int32)[:, None]
    member = ((position >= piece_starts[None, :]) & (position < piece_ends[None, :])).astype(
        jnp.float32
    )
    stacked = (member[:, :, None] * rot_out_rows[:, None, :]).reshape(
        tokens_here, pieces * rank_slice
    )
    grad_rows = lax.dot_general(stacked, rot_in, (((0,), (0,)), ((), ())), precision=highest)
    grad_rows = grad_rows.reshape(pieces, rank_slice, rank_in)
    preceding = from_behind(grad_rows[pieces - 1], "dp", 1)
    joined_next = jnp.where(data_index < data_count - 1, continues[data_index], 0).astype(
        jnp.float32
    )
    joined_prev = jnp.where(data_index > 0, continues[jnp.maximum(data_index - 1, 0)], 0).astype(
        jnp.float32
    )
    grad_rows = grad_rows.at[0].add(joined_prev * preceding)
    grad_rows = grad_rows.at[pieces - 1].multiply(1.0 - joined_next)
    self_part = jnp.sum(grad_rows * grad_rows * scale_block[None], axis=(1, 2))
    grad_low = grad_rows.astype(jnp.bfloat16)

    part = lax.dot_general(
        grad_low, query_grad, (((1, 2), (1, 2)), ((), ())), preferred_element_type=jnp.float32
    )
    part = bit_reversed(part.T, data_count).T

    totals = butterfly_sum(jnp.concatenate([part, self_part[:, None]], axis=1), "factor")
    relative = totals[:, :-1] / jnp.sqrt(totals[:, -1:] + EPSILON)
    relative_all = butterfly_gather(relative, "dp")

    own_all = owners[:, 0]
    doc_count = own_all.shape[0]
    numbers = jnp.arange(doc_count, dtype=jnp.int32)
    earlier = (own_all[None, :] == own_all[:, None]) & (numbers[None, :] < numbers[:, None])
    rank_all = jnp.sum(earlier.astype(jnp.int32), axis=1)
    slots = jnp.arange(OWN_CAP, dtype=jnp.int32)[:, None]
    own_arrived = bit_reversed(own_all, data_count)
    rank_arrived = bit_reversed(rank_all, data_count)
    placing = ((own_arrived[None, :] == data_index) & (rank_arrived[None, :] == slots)).astype(
        jnp.float32
    )
    return jnp.dot(placing, relative_all, precision=highest)


def solution(mesh):
    placed = (
        P("dp", "factor"),
        P("dp", "factor"),
        P("factor", None),
        P("factor", None),
        P(),
        P(),
        P("factor", None),
        P("dp", None, None),
        P("dp", None, None),
        P("dp", None),
        P(),
        P(),
    )
    return jax.shard_map(
        per_device, mesh=mesh, in_specs=placed, out_specs=P("dp", None), check_vma=False
    )
```

```python
import jax
import jax.numpy as jnp
from jax import lax
from jax.sharding import PartitionSpec as P

OWN_CAP = 32


DAMPING = 0.1
EPSILON = 1e-06


def from_behind(block, axis, distance):
    devices = range(lax.axis_size(axis))
    route = [(i - distance, i) for i in devices if i - distance in devices]
    return lax.ppermute(block, axis, route)


def butterfly_sum(block, axis):
    size = lax.axis_size(axis)
    step = 1
    while step < size:
        block = block + lax.ppermute(block, axis, [(i, i ^ step) for i in range(size)])
        step *= 2
    return block


def butterfly_gather(block, axis):
    size = lax.axis_size(axis)
    me = lax.axis_index(axis)
    step = size // 2
    while step >= 1:
        other = lax.ppermute(block, axis, [(i, i ^ step) for i in range(size)])
        upper = (me // step) % 2 == 1
        block = jnp.where(
            upper,
            jnp.concatenate([other, block], axis=0),
            jnp.concatenate([block, other], axis=0),
        )
        step //= 2
    return block


def bit_reversed(rows, count):
    bits = count.bit_length() - 1
    shaped = rows.reshape((2,) * bits + (rows.shape[0] // count,) + rows.shape[1:])
    twisted = tuple(range(bits - 1, -1, -1)) + tuple(range(bits, shaped.ndim))
    return shaped.transpose(twisted).reshape(rows.shape)


def per_device(
    activations,
    out_grads,
    proj_in,
    proj_out,
    basis_in,
    basis_out,
    eigen_values,
    query_in,
    query_out,
    lengths,
    continues,
    owners,
):
    tokens_here = activations.shape[0]
    pieces = lengths.shape[1]
    rank_slice = eigen_values.shape[0]
    rank_in = basis_in.shape[0]
    rank_out = basis_out.shape[0]
    factor_index = lax.axis_index("factor")
    factor_count = lax.axis_size("factor")
    data_index = lax.axis_index("dp")
    data_count = lax.axis_size("dp")
    highest = lax.Precision.HIGHEST
    chunk = tokens_here // factor_count
    scale_block = 1.0 / (eigen_values + DAMPING)
    queries = butterfly_gather(jnp.concatenate([query_in, query_out], axis=2), "dp")


    basis_in_wide = basis_in.astype(jnp.float32)
    basis_out_wide = basis_out.astype(jnp.float32)
    in_part = jnp.dot(activations, proj_in, preferred_element_type=jnp.float32)
    out_part = jnp.dot(out_grads, proj_out, preferred_element_type=jnp.float32)
    stacked_parts = jnp.concatenate([in_part, out_part], axis=1)
    gathered_parts = lax.all_to_all(stacked_parts, "factor", 0, 0, tiled=True)
    basis_cut = lax.dynamic_slice_in_dim(basis_out_wide, factor_index * rank_slice, rank_slice, 1)
    q_in = jnp.einsum(
        "qtk,kl->qtl", queries[:, :, :rank_in].astype(jnp.float32), basis_in_wide, precision=highest
    )
    q_out = jnp.einsum(
        "qtk,kl->qtl", queries[:, :, rank_in:].astype(jnp.float32), basis_cut, precision=highest
    )
    outer = jnp.einsum("qti,qtj->qij", q_out, q_in, precision=highest)
    query_grad = (outer * scale_block[None]).astype(jnp.bfloat16)
    chunk_sums = jnp.sum(gathered_parts.reshape(factor_count, chunk, rank_in + rank_out), axis=0)
    rot_in_chunk = jnp.dot(chunk_sums[:, :rank_in], basis_in_wide, precision=highest)
    rot_out_chunk = jnp.dot(chunk_sums[:, rank_in:], basis_out_wide, precision=highest)
    out_blocks = rot_out_chunk.reshape(chunk, factor_count, rank_slice).transpose(1, 0, 2)
    sending = jnp.concatenate(
        [jnp.broadcast_to(rot_in_chunk[None], (factor_count, chunk, rank_in)), out_blocks], axis=2
    ).reshape(factor_count * chunk, rank_in + rank_slice)
    received = lax.all_to_all(sending, "factor", 0, 0, tiled=True)
    received, query_grad = lax.optimization_barrier((received, query_grad))
    rot_in = received[:, :rank_in]
    rot_out_rows = received[:, rank_in:]

    piece_lengths = lengths[0]
    piece_ends = jnp.cumsum(piece_lengths)
    piece_starts = piece_ends - piece_lengths
    position = jnp.arange(tokens_here, dtype=jnp.int32)[:, None]
    member = ((position >= piece_starts[None, :]) & (position < piece_ends[None, :])).astype(
        jnp.float32
    )
    stacked = (member[:, :, None] * rot_out_rows[:, None, :]).reshape(
        tokens_here, pieces * rank_slice
    )
    grad_rows = lax.dot_general(stacked, rot_in, (((0,), (0,)), ((), ())), precision=highest)
    grad_rows = grad_rows.reshape(pieces, rank_slice, rank_in)
    preceding = from_behind(grad_rows[pieces - 1], "dp", 1)
    joined_next = jnp.where(data_index < data_count - 1, continues[data_index], 0).astype(
        jnp.float32
    )
    joined_prev = jnp.where(data_index > 0, continues[jnp.maximum(data_index - 1, 0)], 0).astype(
        jnp.float32
    )
    grad_rows = grad_rows.at[0].add(joined_prev * preceding)
    grad_rows = grad_rows.at[pieces - 1].multiply(1.0 - joined_next)
    self_part = jnp.sum(grad_rows * grad_rows * scale_block[None], axis=(1, 2))
    grad_low = grad_rows.astype(jnp.bfloat16)

    part = lax.dot_general(
        grad_low, query_grad, (((1, 2), (1, 2)), ((), ())), preferred_element_type=jnp.float32
    )
    part = bit_reversed(part.T, data_count).T

    totals = butterfly_sum(jnp.concatenate([part, self_part[:, None]], axis=1), "factor")
    relative = totals[:, :-1] / jnp.sqrt(totals[:, -1:] + EPSILON)
    relative_all = butterfly_gather(relative, "dp")

    own_all = owners[:, 0]
    doc_count = own_all.shape[0]
    numbers = jnp.arange(doc_count, dtype=jnp.int32)
    earlier = (own_all[None, :] == own_all[:, None]) & (numbers[None, :] < numbers[:, None])
    rank_all = jnp.sum(earlier.astype(jnp.int32), axis=1)
    slots = jnp.arange(OWN_CAP, dtype=jnp.int32)[:, None]
    own_arrived = bit_reversed(own_all, data_count)
    rank_arrived = bit_reversed(rank_all, data_count)
    placing = ((own_arrived[None, :] == data_index) & (rank_arrived[None, :] == slots)).astype(
        jnp.float32
    )
    return jnp.dot(placing, relative_all, precision=highest)


def solution(mesh):
    placed = (
        P("dp", "factor"),
        P("dp", "factor"),
        P("factor", None),
        P("factor", None),
        P(),
        P(),
        P("factor", None),
        P("dp", None, None),
        P("dp", None, None),
        P("dp", None),
        P(),
        P(),
    )
    return jax.shard_map(
        per_device, mesh=mesh, in_specs=placed, out_specs=P("dp", None), check_vma=False
    )
```

```python
import jax
import jax.numpy as jnp
from jax import lax
from jax.sharding import PartitionSpec as P

OWN_CAP = 32


DAMPING = 0.1
EPSILON = 1e-06


def from_behind(block, axis, distance):
    devices = range(lax.axis_size(axis))
    route = [(i - distance, i) for i in devices if i - distance in devices]
    return lax.ppermute(block, axis, route)


def butterfly_sum(block, axis):
    size = lax.axis_size(axis)
    step = 1
    while step < size:
        block = block + lax.ppermute(block, axis, [(i, i ^ step) for i in range(size)])
        step *= 2
    return block


def butterfly_gather(block, axis, bits):
    size = lax.axis_size(axis)
    me = lax.axis_index(axis)
    for bit in bits:
        step = 1 << bit
        other = lax.ppermute(block, axis, [(i, i ^ step) for i in range(size)])
        upper = (me // step) % 2 == 1
        block = jnp.where(
            upper,
            jnp.concatenate([other, block], axis=0),
            jnp.concatenate([block, other], axis=0),
        )
    return block


def arrival_axes(bits):
    top = len(bits) - 1
    return tuple(top - bit for bit in reversed(bits))


def to_arrival(rows, bits):
    count = 1 << len(bits)
    shaped = rows.reshape((2,) * len(bits) + (rows.shape[0] // count,) + rows.shape[1:])
    axes = arrival_axes(bits) + tuple(range(len(bits), shaped.ndim))
    return shaped.transpose(axes).reshape(rows.shape)


def from_arrival(rows, bits):
    count = 1 << len(bits)
    shaped = rows.reshape((2,) * len(bits) + (rows.shape[0] // count,) + rows.shape[1:])
    forward = arrival_axes(bits)
    back = tuple(forward.index(i) for i in range(len(bits)))
    axes = back + tuple(range(len(bits), shaped.ndim))
    return shaped.transpose(axes).reshape(rows.shape)


def per_device(
    activations,
    out_grads,
    proj_in,
    proj_out,
    basis_in,
    basis_out,
    eigen_values,
    query_in,
    query_out,
    lengths,
    continues,
    owners,
):
    tokens_here = activations.shape[0]
    pieces = lengths.shape[1]
    rank_slice = eigen_values.shape[0]
    rank_in = basis_in.shape[0]
    rank_out = basis_out.shape[0]
    factor_index = lax.axis_index("factor")
    factor_count = lax.axis_size("factor")
    data_index = lax.axis_index("dp")
    data_count = lax.axis_size("dp")
    highest = lax.Precision.HIGHEST
    chunk = tokens_here // factor_count
    scale_block = 1.0 / (eigen_values + DAMPING)
    data_bits = data_count.bit_length() - 1
    query_bits = (1,) + tuple(range(data_bits - 1, 1, -1)) + (0,)
    score_bits = tuple(range(data_bits - 1, -1, -1))
    queries = butterfly_gather(jnp.concatenate([query_in, query_out], axis=2), "dp", query_bits)


    basis_in_wide = basis_in.astype(jnp.float32)
    basis_out_wide = basis_out.astype(jnp.float32)
    in_part = jnp.dot(activations, proj_in, preferred_element_type=jnp.float32)
    out_part = jnp.dot(out_grads, proj_out, preferred_element_type=jnp.float32)
    stacked_parts = jnp.concatenate([in_part, out_part], axis=1)
    gathered_parts = lax.all_to_all(stacked_parts, "factor", 0, 0, tiled=True)
    basis_cut = lax.dynamic_slice_in_dim(basis_out_wide, factor_index * rank_slice, rank_slice, 1)
    q_in = jnp.einsum(
        "qtk,kl->qtl", queries[:, :, :rank_in].astype(jnp.float32), basis_in_wide, precision=highest
    )
    q_out = jnp.einsum(
        "qtk,kl->qtl", queries[:, :, rank_in:].astype(jnp.float32), basis_cut, precision=highest
    )
    outer = jnp.einsum("qti,qtj->qij", q_out, q_in, precision=highest)
    query_grad = (outer * scale_block[None]).astype(jnp.bfloat16)
    chunk_sums = jnp.sum(gathered_parts.reshape(factor_count, chunk, rank_in + rank_out), axis=0)
    rot_in_chunk = jnp.dot(chunk_sums[:, :rank_in], basis_in_wide, precision=highest)
    rot_out_chunk = jnp.dot(chunk_sums[:, rank_in:], basis_out_wide, precision=highest)
    out_blocks = rot_out_chunk.reshape(chunk, factor_count, rank_slice).transpose(1, 0, 2)
    sending = jnp.concatenate(
        [jnp.broadcast_to(rot_in_chunk[None], (factor_count, chunk, rank_in)), out_blocks], axis=2
    ).reshape(factor_count * chunk, rank_in + rank_slice)
    received = lax.all_to_all(sending, "factor", 0, 0, tiled=True)
    rot_in = received[:, :rank_in]
    rot_out_rows = received[:, rank_in:]

    piece_lengths = lengths[0]
    piece_ends = jnp.cumsum(piece_lengths)
    piece_starts = piece_ends - piece_lengths
    position = jnp.arange(tokens_here, dtype=jnp.int32)[:, None]
    member = ((position >= piece_starts[None, :]) & (position < piece_ends[None, :])).astype(
        jnp.float32
    )
    stacked = (member[:, :, None] * rot_out_rows[:, None, :]).reshape(
        tokens_here, pieces * rank_slice
    )
    grad_rows = lax.dot_general(stacked, rot_in, (((0,), (0,)), ((), ())), precision=highest)
    grad_rows = grad_rows.reshape(pieces, rank_slice, rank_in)
    preceding = from_behind(grad_rows[pieces - 1], "dp", 1)
    joined_next = jnp.where(data_index < data_count - 1, continues[data_index], 0).astype(
        jnp.float32
    )
    joined_prev = jnp.where(data_index > 0, continues[jnp.maximum(data_index - 1, 0)], 0).astype(
        jnp.float32
    )
    grad_rows = grad_rows.at[0].add(joined_prev * preceding)
    grad_rows = grad_rows.at[pieces - 1].multiply(1.0 - joined_next)
    self_part = jnp.sum(grad_rows * grad_rows * scale_block[None], axis=(1, 2))
    grad_low = grad_rows.astype(jnp.bfloat16)

    part = lax.dot_general(
        grad_low, query_grad, (((1, 2), (1, 2)), ((), ())), preferred_element_type=jnp.float32
    )
    part = from_arrival(part.T, query_bits).T

    totals = butterfly_sum(jnp.concatenate([part, self_part[:, None]], axis=1), "factor")
    relative = totals[:, :-1] / jnp.sqrt(totals[:, -1:] + EPSILON)
    relative_all = butterfly_gather(relative, "dp", score_bits)

    own_all = owners[:, 0]
    doc_count = own_all.shape[0]
    numbers = jnp.arange(doc_count, dtype=jnp.int32)
    earlier = (own_all[None, :] == own_all[:, None]) & (numbers[None, :] < numbers[:, None])
    rank_all = jnp.sum(earlier.astype(jnp.int32), axis=1)
    slots = jnp.arange(OWN_CAP, dtype=jnp.int32)[:, None]
    own_arrived = to_arrival(own_all, score_bits)
    rank_arrived = to_arrival(rank_all, score_bits)
    placing = ((own_arrived[None, :] == data_index) & (rank_arrived[None, :] == slots)).astype(
        jnp.float32
    )
    return jnp.dot(placing, relative_all, precision=highest)


def solution(mesh):
    placed = (
        P("dp", "factor"),
        P("dp", "factor"),
        P("factor", None),
        P("factor", None),
        P(),
        P(),
        P("factor", None),
        P("dp", None, None),
        P("dp", None, None),
        P("dp", None),
        P(),
        P(),
    )
    return jax.shard_map(
        per_device, mesh=mesh, in_specs=placed, out_specs=P("dp", None), check_vma=False
    )
```

```python
import jax
import jax.numpy as jnp
from jax import lax
from jax.sharding import PartitionSpec as P

OWN_CAP = 32


DAMPING = 0.1
EPSILON = 1e-06


def from_behind(block, axis, distance):
    devices = range(lax.axis_size(axis))
    route = [(i - distance, i) for i in devices if i - distance in devices]
    return lax.ppermute(block, axis, route)


def butterfly_sum(block, axis):
    size = lax.axis_size(axis)
    step = 1
    while step < size:
        block = block + lax.ppermute(block, axis, [(i, i ^ step) for i in range(size)])
        step *= 2
    return block


def butterfly_gather(block, axis):
    size = lax.axis_size(axis)
    me = lax.axis_index(axis)
    step = size // 2
    while step >= 1:
        other = lax.ppermute(block, axis, [(i, i ^ step) for i in range(size)])
        upper = (me // step) % 2 == 1
        block = jnp.where(
            upper,
            jnp.concatenate([other, block], axis=0),
            jnp.concatenate([block, other], axis=0),
        )
        step //= 2
    return block


def bit_reversed(rows, count):
    bits = count.bit_length() - 1
    shaped = rows.reshape((2,) * bits + (rows.shape[0] // count,) + rows.shape[1:])
    twisted = tuple(range(bits - 1, -1, -1)) + tuple(range(bits, shaped.ndim))
    return shaped.transpose(twisted).reshape(rows.shape)


def per_device(
    activations,
    out_grads,
    proj_in,
    proj_out,
    basis_in,
    basis_out,
    eigen_values,
    query_in,
    query_out,
    lengths,
    continues,
    owners,
):
    tokens_here = activations.shape[0]
    pieces = lengths.shape[1]
    rank_slice = eigen_values.shape[0]
    rank_in = basis_in.shape[0]
    rank_out = basis_out.shape[0]
    factor_index = lax.axis_index("factor")
    factor_count = lax.axis_size("factor")
    data_index = lax.axis_index("dp")
    data_count = lax.axis_size("dp")
    highest = lax.Precision.HIGHEST
    chunk = tokens_here // factor_count
    scale_block = 1.0 / (eigen_values + DAMPING)
    queries = butterfly_gather(jnp.concatenate([query_in, query_out], axis=2), "dp")


    basis_in_wide = basis_in.astype(jnp.float32)
    basis_out_wide = basis_out.astype(jnp.float32)
    in_part = jnp.dot(activations, proj_in, preferred_element_type=jnp.float32)
    out_part = jnp.dot(out_grads, proj_out, preferred_element_type=jnp.float32)
    out_sums = jnp.sum(
        lax.all_to_all(out_part, "factor", 0, 0, tiled=True).reshape(factor_count, chunk, rank_out), axis=0
    )
    in_sums = jnp.sum(
        lax.all_to_all(in_part, "factor", 0, 0, tiled=True).reshape(factor_count, chunk, rank_in), axis=0
    )
    basis_cut = lax.dynamic_slice_in_dim(basis_out_wide, factor_index * rank_slice, rank_slice, 1)
    q_in = jnp.einsum(
        "qtk,kl->qtl", queries[:, :, :rank_in].astype(jnp.float32), basis_in_wide, precision=highest
    )
    q_out = jnp.einsum(
        "qtk,kl->qtl", queries[:, :, rank_in:].astype(jnp.float32), basis_cut, precision=highest
    )
    outer = jnp.einsum("qti,qtj->qij", q_out, q_in, precision=highest)
    query_grad = (outer * scale_block[None]).astype(jnp.bfloat16)
    rot_in_chunk = jnp.dot(in_sums, basis_in_wide, precision=highest)
    rot_out_chunk = jnp.dot(out_sums, basis_out_wide, precision=highest)
    out_blocks = rot_out_chunk.reshape(chunk, factor_count, rank_slice).transpose(1, 0, 2)
    sending = jnp.concatenate(
        [jnp.broadcast_to(rot_in_chunk[None], (factor_count, chunk, rank_in)), out_blocks], axis=2
    ).reshape(factor_count * chunk, rank_in + rank_slice)
    received = lax.all_to_all(sending, "factor", 0, 0, tiled=True)
    rot_in = received[:, :rank_in]
    rot_out_rows = received[:, rank_in:]

    piece_lengths = lengths[0]
    piece_ends = jnp.cumsum(piece_lengths)
    piece_starts = piece_ends - piece_lengths
    position = jnp.arange(tokens_here, dtype=jnp.int32)[:, None]
    member = ((position >= piece_starts[None, :]) & (position < piece_ends[None, :])).astype(
        jnp.float32
    )
    stacked = (member[:, :, None] * rot_out_rows[:, None, :]).reshape(
        tokens_here, pieces * rank_slice
    )
    grad_rows = lax.dot_general(stacked, rot_in, (((0,), (0,)), ((), ())), precision=highest)
    grad_rows = grad_rows.reshape(pieces, rank_slice, rank_in)
    preceding = from_behind(grad_rows[pieces - 1], "dp", 1)
    joined_next = jnp.where(data_index < data_count - 1, continues[data_index], 0).astype(
        jnp.float32
    )
    joined_prev = jnp.where(data_index > 0, continues[jnp.maximum(data_index - 1, 0)], 0).astype(
        jnp.float32
    )
    grad_rows = grad_rows.at[0].add(joined_prev * preceding)
    grad_rows = grad_rows.at[pieces - 1].multiply(1.0 - joined_next)
    self_part = jnp.sum(grad_rows * grad_rows * scale_block[None], axis=(1, 2))
    grad_low = grad_rows.astype(jnp.bfloat16)

    part = lax.dot_general(
        grad_low, query_grad, (((1, 2), (1, 2)), ((), ())), preferred_element_type=jnp.float32
    )
    part = bit_reversed(part.T, data_count).T

    totals = butterfly_sum(jnp.concatenate([part, self_part[:, None]], axis=1), "factor")
    relative = totals[:, :-1] / jnp.sqrt(totals[:, -1:] + EPSILON)
    relative_all = butterfly_gather(relative, "dp")

    own_all = owners[:, 0]
    doc_count = own_all.shape[0]
    numbers = jnp.arange(doc_count, dtype=jnp.int32)
    earlier = (own_all[None, :] == own_all[:, None]) & (numbers[None, :] < numbers[:, None])
    rank_all = jnp.sum(earlier.astype(jnp.int32), axis=1)
    slots = jnp.arange(OWN_CAP, dtype=jnp.int32)[:, None]
    own_arrived = bit_reversed(own_all, data_count)
    rank_arrived = bit_reversed(rank_all, data_count)
    placing = ((own_arrived[None, :] == data_index) & (rank_arrived[None, :] == slots)).astype(
        jnp.float32
    )
    return jnp.dot(placing, relative_all, precision=highest)


def solution(mesh):
    placed = (
        P("dp", "factor"),
        P("dp", "factor"),
        P("factor", None),
        P("factor", None),
        P(),
        P(),
        P("factor", None),
        P("dp", None, None),
        P("dp", None, None),
        P("dp", None),
        P(),
        P(),
    )
    return jax.shard_map(
        per_device, mesh=mesh, in_specs=placed, out_specs=P("dp", None), check_vma=False
    )
```

```python
import jax
import jax.numpy as jnp
from jax import lax
from jax.sharding import PartitionSpec as P

OWN_CAP = 32


DAMPING = 0.1
EPSILON = 1e-06


def from_behind(block, axis, distance):
    devices = range(lax.axis_size(axis))
    route = [(i - distance, i) for i in devices if i - distance in devices]
    return lax.ppermute(block, axis, route)


def butterfly_sum(block, axis):
    size = lax.axis_size(axis)
    step = 1
    while step < size:
        block = block + lax.ppermute(block, axis, [(i, i ^ step) for i in range(size)])
        step *= 2
    return block


def butterfly_gather(block, axis):
    size = lax.axis_size(axis)
    me = lax.axis_index(axis)
    step = size // 2
    while step >= 1:
        other = lax.ppermute(block, axis, [(i, i ^ step) for i in range(size)])
        upper = (me // step) % 2 == 1
        block = jnp.where(
            upper,
            jnp.concatenate([other, block], axis=0),
            jnp.concatenate([block, other], axis=0),
        )
        step //= 2
    return block


def bit_reversed(rows, count):
    bits = count.bit_length() - 1
    shaped = rows.reshape((2,) * bits + (rows.shape[0] // count,) + rows.shape[1:])
    twisted = tuple(range(bits - 1, -1, -1)) + tuple(range(bits, shaped.ndim))
    return shaped.transpose(twisted).reshape(rows.shape)


def per_device(
    activations,
    out_grads,
    proj_in,
    proj_out,
    basis_in,
    basis_out,
    eigen_values,
    query_in,
    query_out,
    lengths,
    continues,
    owners,
):
    tokens_here = activations.shape[0]
    pieces = lengths.shape[1]
    rank_slice = eigen_values.shape[0]
    rank_in = basis_in.shape[0]
    rank_out = basis_out.shape[0]
    factor_index = lax.axis_index("factor")
    factor_count = lax.axis_size("factor")
    data_index = lax.axis_index("dp")
    data_count = lax.axis_size("dp")
    highest = lax.Precision.HIGHEST
    chunk = tokens_here // factor_count
    scale_block = 1.0 / (eigen_values + DAMPING)
    queries = butterfly_gather(jnp.concatenate([query_in, query_out], axis=2), "dp")


    basis_in_wide = basis_in.astype(jnp.float32)
    basis_out_wide = basis_out.astype(jnp.float32)
    in_part = jnp.dot(activations, proj_in, preferred_element_type=jnp.float32)
    out_part = jnp.dot(out_grads, proj_out, preferred_element_type=jnp.float32)
    stacked_parts = jnp.concatenate([in_part, out_part], axis=1)
    gathered_parts = lax.all_to_all(stacked_parts, "factor", 0, 0, tiled=True)
    basis_cut = lax.dynamic_slice_in_dim(basis_out_wide, factor_index * rank_slice, rank_slice, 1)
    q_in = jnp.einsum(
        "qtk,kl->qtl", queries[:, :, :rank_in].astype(jnp.float32), basis_in_wide, precision=highest
    )
    q_out = jnp.einsum(
        "qtk,kl->qtl", queries[:, :, rank_in:].astype(jnp.float32), basis_cut, precision=highest
    )
    outer = jnp.einsum("qti,qtj->qij", q_out, q_in, precision=highest)
    query_grad = (outer * scale_block[None]).astype(jnp.bfloat16)
    chunk_sums = jnp.sum(gathered_parts.reshape(factor_count, chunk, rank_in + rank_out), axis=0)
    rot_in_chunk = jnp.dot(chunk_sums[:, :rank_in], basis_in_wide, precision=highest)
    rot_out_chunk = jnp.dot(chunk_sums[:, rank_in:], basis_out_wide, precision=highest)
    out_blocks = rot_out_chunk.reshape(chunk, factor_count, rank_slice).transpose(1, 0, 2)
    sending = jnp.concatenate(
        [jnp.broadcast_to(rot_in_chunk[None], (factor_count, chunk, rank_in)), out_blocks], axis=2
    ).reshape(factor_count * chunk, rank_in + rank_slice)
    received = lax.all_to_all(sending, "factor", 0, 0, tiled=True)
    rot_in = received[:, :rank_in]
    rot_out_rows = received[:, rank_in:]

    piece_lengths = lengths[0]
    piece_ends = jnp.cumsum(piece_lengths)
    piece_starts = piece_ends - piece_lengths
    position = jnp.arange(tokens_here, dtype=jnp.int32)[:, None]
    member = ((position >= piece_starts[None, :]) & (position < piece_ends[None, :])).astype(
        jnp.float32
    )
    stacked = (member[:, :, None] * rot_out_rows[:, None, :]).reshape(
        tokens_here, pieces * rank_slice
    )
    grad_rows = lax.dot_general(stacked, rot_in, (((0,), (0,)), ((), ())), precision=highest)
    grad_rows = grad_rows.reshape(pieces, rank_slice, rank_in)
    preceding = from_behind(grad_rows[pieces - 1], "dp", 1)
    joined_next = jnp.where(data_index < data_count - 1, continues[data_index], 0).astype(
        jnp.float32
    )
    joined_prev = jnp.where(data_index > 0, continues[jnp.maximum(data_index - 1, 0)], 0).astype(
        jnp.float32
    )
    grad_rows = grad_rows.at[0].add(joined_prev * preceding)
    grad_rows = grad_rows.at[pieces - 1].multiply(1.0 - joined_next)
    self_part = jnp.sum(grad_rows * grad_rows * scale_block[None], axis=(1, 2))
    grad_low = grad_rows.astype(jnp.bfloat16)

    part_by_query = lax.dot_general(
        query_grad, grad_low, (((1, 2), (1, 2)), ((), ())), preferred_element_type=jnp.float32
    )
    part = bit_reversed(part_by_query, data_count).T

    totals = butterfly_sum(jnp.concatenate([part, self_part[:, None]], axis=1), "factor")
    relative = totals[:, :-1] / jnp.sqrt(totals[:, -1:] + EPSILON)
    relative_all = butterfly_gather(relative, "dp")

    own_all = owners[:, 0]
    doc_count = own_all.shape[0]
    numbers = jnp.arange(doc_count, dtype=jnp.int32)
    earlier = (own_all[None, :] == own_all[:, None]) & (numbers[None, :] < numbers[:, None])
    rank_all = jnp.sum(earlier.astype(jnp.int32), axis=1)
    slots = jnp.arange(OWN_CAP, dtype=jnp.int32)[:, None]
    own_arrived = bit_reversed(own_all, data_count)
    rank_arrived = bit_reversed(rank_all, data_count)
    placing = ((own_arrived[None, :] == data_index) & (rank_arrived[None, :] == slots)).astype(
        jnp.float32
    )
    return jnp.dot(placing, relative_all, precision=highest)


def solution(mesh):
    placed = (
        P("dp", "factor"),
        P("dp", "factor"),
        P("factor", None),
        P("factor", None),
        P(),
        P(),
        P("factor", None),
        P("dp", None, None),
        P("dp", None, None),
        P("dp", None),
        P(),
        P(),
    )
    return jax.shard_map(
        per_device, mesh=mesh, in_specs=placed, out_specs=P("dp", None), check_vma=False
    )
```

```python
import jax
import jax.numpy as jnp
from jax import lax
from jax.sharding import PartitionSpec as P

OWN_CAP = 32


DAMPING = 0.1
EPSILON = 1e-06


def from_behind(block, axis, distance):
    devices = range(lax.axis_size(axis))
    route = [(i - distance, i) for i in devices if i - distance in devices]
    return lax.ppermute(block, axis, route)


def butterfly_sum(block, axis):
    size = lax.axis_size(axis)
    step = 1
    while step < size:
        block = block + lax.ppermute(block, axis, [(i, i ^ step) for i in range(size)])
        step *= 2
    return block


def butterfly_gather(block, axis):
    size = lax.axis_size(axis)
    me = lax.axis_index(axis)
    step = size // 2
    while step >= 1:
        other = lax.ppermute(block, axis, [(i, i ^ step) for i in range(size)])
        upper = (me // step) % 2 == 1
        block = jnp.where(
            upper,
            jnp.concatenate([other, block], axis=0),
            jnp.concatenate([block, other], axis=0),
        )
        step //= 2
    return block


def bit_reversed(rows, count):
    bits = count.bit_length() - 1
    shaped = rows.reshape((2,) * bits + (rows.shape[0] // count,) + rows.shape[1:])
    twisted = tuple(range(bits - 1, -1, -1)) + tuple(range(bits, shaped.ndim))
    return shaped.transpose(twisted).reshape(rows.shape)


def per_device(
    activations,
    out_grads,
    proj_in,
    proj_out,
    basis_in,
    basis_out,
    eigen_values,
    query_in,
    query_out,
    lengths,
    continues,
    owners,
):
    tokens_here = activations.shape[0]
    pieces = lengths.shape[1]
    rank_slice = eigen_values.shape[0]
    rank_in = basis_in.shape[0]
    rank_out = basis_out.shape[0]
    factor_index = lax.axis_index("factor")
    factor_count = lax.axis_size("factor")
    data_index = lax.axis_index("dp")
    data_count = lax.axis_size("dp")
    highest = lax.Precision.HIGHEST
    chunk = tokens_here // factor_count
    scale_block = 1.0 / (eigen_values + DAMPING)
    queries = butterfly_gather(jnp.concatenate([query_in, query_out], axis=2), "dp")


    basis_in_wide = basis_in.astype(jnp.float32)
    basis_out_wide = basis_out.astype(jnp.float32)
    in_part = jnp.dot(activations, proj_in, preferred_element_type=jnp.float32)
    out_part = jnp.dot(out_grads, proj_out, preferred_element_type=jnp.float32)
    stacked_parts = jnp.concatenate([in_part, out_part], axis=1)
    gathered_parts = lax.all_to_all(stacked_parts, "factor", 0, 0, tiled=True)
    basis_cut = lax.dynamic_slice_in_dim(basis_out_wide, factor_index * rank_slice, rank_slice, 1)
    q_in = jnp.einsum(
        "qtk,kl->qtl", queries[:, :, :rank_in].astype(jnp.float32), basis_in_wide, precision=highest
    )
    q_out = jnp.einsum(
        "qtk,kl->qtl", queries[:, :, rank_in:].astype(jnp.float32), basis_cut, precision=highest
    )
    outer = jnp.einsum("qti,qtj->qij", q_out, q_in, precision=highest)
    query_grad = (outer * scale_block[None]).astype(jnp.bfloat16)
    chunk_sums = jnp.sum(gathered_parts.reshape(factor_count, chunk, rank_in + rank_out), axis=0)
    rot_in_chunk = jnp.dot(chunk_sums[:, :rank_in], basis_in_wide, precision=highest)
    rot_out_chunk = jnp.dot(chunk_sums[:, rank_in:], basis_out_wide, precision=highest)
    out_blocks = rot_out_chunk.reshape(chunk, factor_count, rank_slice).transpose(1, 2, 0)
    sending = jnp.concatenate(
        [jnp.broadcast_to(rot_in_chunk[None], (factor_count, chunk, rank_in)), out_blocks], axis=1
    )
    received = lax.all_to_all(sending, "factor", 0, 0, tiled=True)
    rot_in = received[:, :chunk, :].reshape(tokens_here, rank_in)
    rot_out_cols = received[:, chunk:, :].transpose(1, 0, 2).reshape(rank_slice, tokens_here)

    piece_lengths = lengths[0]
    piece_ends = jnp.cumsum(piece_lengths)
    piece_starts = piece_ends - piece_lengths
    position = jnp.arange(tokens_here, dtype=jnp.int32)[:, None]
    member = ((position >= piece_starts[None, :]) & (position < piece_ends[None, :])).astype(
        jnp.float32
    )
    stacked = (member.T[:, None, :] * rot_out_cols[None, :, :]).reshape(
        pieces * rank_slice, tokens_here
    )
    grad_rows = jnp.dot(stacked, rot_in, precision=highest)
    grad_rows = grad_rows.reshape(pieces, rank_slice, rank_in)
    preceding = from_behind(grad_rows[pieces - 1], "dp", 1)
    joined_next = jnp.where(data_index < data_count - 1, continues[data_index], 0).astype(
        jnp.float32
    )
    joined_prev = jnp.where(data_index > 0, continues[jnp.maximum(data_index - 1, 0)], 0).astype(
        jnp.float32
    )
    grad_rows = grad_rows.at[0].add(joined_prev * preceding)
    grad_rows = grad_rows.at[pieces - 1].multiply(1.0 - joined_next)
    self_part = jnp.sum(grad_rows * grad_rows * scale_block[None], axis=(1, 2))
    grad_low = grad_rows.astype(jnp.bfloat16)

    part = lax.dot_general(
        grad_low, query_grad, (((1, 2), (1, 2)), ((), ())), preferred_element_type=jnp.float32
    )
    part = bit_reversed(part.T, data_count).T

    totals = butterfly_sum(jnp.concatenate([part, self_part[:, None]], axis=1), "factor")
    relative = totals[:, :-1] / jnp.sqrt(totals[:, -1:] + EPSILON)
    relative_all = butterfly_gather(relative, "dp")

    own_all = owners[:, 0]
    doc_count = own_all.shape[0]
    numbers = jnp.arange(doc_count, dtype=jnp.int32)
    earlier = (own_all[None, :] == own_all[:, None]) & (numbers[None, :] < numbers[:, None])
    rank_all = jnp.sum(earlier.astype(jnp.int32), axis=1)
    slots = jnp.arange(OWN_CAP, dtype=jnp.int32)[:, None]
    own_arrived = bit_reversed(own_all, data_count)
    rank_arrived = bit_reversed(rank_all, data_count)
    placing = ((own_arrived[None, :] == data_index) & (rank_arrived[None, :] == slots)).astype(
        jnp.float32
    )
    return jnp.dot(placing, relative_all, precision=highest)


def solution(mesh):
    placed = (
        P("dp", "factor"),
        P("dp", "factor"),
        P("factor", None),
        P("factor", None),
        P(),
        P(),
        P("factor", None),
        P("dp", None, None),
        P("dp", None, None),
        P("dp", None),
        P(),
        P(),
    )
    return jax.shard_map(
        per_device, mesh=mesh, in_specs=placed, out_specs=P("dp", None), check_vma=False
    )
```
